512 devices in a mesh: dp: 32 (over x, y, core), expert: 16 (over z).
Axes of the slice: x: 4, y: 4, z: 16, core: 2. Of those that a mesh axis runs over, the one named last changes fastest.
Arguments:
- out_grad: bfloat16 [65536, 2048], P(('dp', 'expert')), may hold values from -6 to 6
- expert_ids: int32 [65536, 4], P(('dp', 'expert')), may hold values from 0 to 15, all different within a row; in each aligned block of 128 rows (0 to 127, 128 to 255, ...) at most 64 rows name the same one
- route_weights: bfloat16 [65536, 4], P(('dp', 'expert')), may hold values from 0.049804688 to 1
- pre_activations: bfloat16 [65536, 4, 1536], P(('dp', 'expert')), may hold values from -6 to 6
- down_weight: bfloat16 [16, 768, 2048], P('expert', 'dp'), may hold values from -0.21875 to 0.21875
Outputs:
- pre_grad: bfloat16 [65536, 4, 1536], P(('dp', 'expert'))
- weight_grad: bfloat16 [65536, 4], P(('dp', 'expert'))
- down_grad: bfloat16 [16, 768, 2048], P('expert', 'dp')
The draws below stay inside these ranges and needn't reach their ends.
Inputs may be any that keep to these rules, and one draw needn't show every extreme that they name: `expert_ids`: among the 128 rows of one device, each expert is named by at most 64 rows, a bound that some block reaches; the numbers in a row are distinct.
All inputs are finite; a program needn't handle non-finite values.
Results may differ from the reference program's by a relative error of at most 0.015.
Values may be sent and summed in bfloat16 or wider, within the bound.
No kernel may reach another device: no remote copies, remote signals or barrier semaphores. Data moves between devices by JAX's collectives and lax.ppermute only.
A program may use at most 64 MiB of HBM per device.

```python
import math
import jax
import jax.numpy as jnp
import numpy as np
from jax import lax

D = 2048
FF = 768
TOP = 4
EXPERTS = 16
TOK_DEV = 128
CAP = 64
TOKENS = 65536
N_DP = 32
N_EXPERT = 16


def steps_of(stream_key, dims, cuts, low, top_value):
    gain, own = 1.0, jax.random.fold_in(stream_key, 6)
    for dim, blocks in cuts:
        heights = jnp.exp(jax.random.uniform(jax.random.fold_in(own, dim), (blocks,), jnp.float32, low / len(cuts), top_value / len(cuts)))
        gain = gain * jnp.repeat(heights, dims[dim] // blocks).reshape([-1 if axis == dim else 1 for axis in range(len(dims))])
    return gain


def deal_out(rng, own, number, rows, amount, top, most, lean):
    order = jax.random.permutation(rng, amount)
    crowded, ordinary = shares(amount, rows * top, most, lean, True), shares(amount, rows * top, most, lean, False)
    places = jnp.arange(amount)

    def named(tallies, turn):
        used = int((tallies > 0).sum())
        fixed = max(1, used // 4)
        passed = fixed + (places - fixed + turn * (used - fixed)) % max(1, amount - fixed)
        return jnp.zeros((amount,), jnp.int32).at[order[jnp.where(places < fixed, places, passed)]].set(jnp.asarray(tallies, jnp.int32))

    tallies = jnp.where(number % 4 == 0, named(crowded, number // 4), named(ordinary, number - number // 4 - 1))
    mixed = jax.random.permutation(jax.random.fold_in(own, 3), amount)
    giver, taker = mixed[0:amount // 2 * 2:2], mixed[1:amount // 2 * 2:2]
    margin = jnp.minimum(tallies[giver] - 1, most - tallies[taker]) // 2
    margin = jnp.where((giver == order[0]) | (taker == order[0]) | (tallies[taker] == 0), 0, jnp.maximum(margin, 0))
    passed = jax.random.randint(jax.random.fold_in(own, 4), (amount // 2,), 0, 1 << 20) % (margin + 1)
    tallies = tallies.at[giver].add(-passed).at[taker].add(passed)
    labels = jnp.searchsorted(jnp.cumsum(tallies), jnp.arange(rows * top), side="right").astype(jnp.int32)
    grid = labels.reshape(top, rows).T
    grid = grid[jax.random.permutation(jax.random.fold_in(own, 1), rows)]
    turn = jax.random.randint(jax.random.fold_in(own, 2), (rows, 1), 0, top)
    return jnp.take_along_axis(grid, (jnp.arange(top)[None, :] + turn) % top, axis=1)


def shares(count, total, limit, lean, full):
    portions = [(1 << 20) // math.isqrt(rank ** lean) + 1 for rank in range(1, count + 1)]
    largest = limit if full else min(limit, max(-(-total // count), total * portions[0] // sum(portions)))
    least = 1 if total - largest >= count - 1 else 0
    counts, spare = [largest] + [least] * (count - 1), total - largest - least * (count - 1)
    while spare > 0:
        candidates = [i for i in range(1, count) if counts[i] < largest] or [i for i in range(1, count) if counts[i] < limit]
        pool, budget = sum([portions[i] for i in candidates]), spare
        for i in candidates:
            extra = min(limit - counts[i], max(1, budget * portions[i] // pool), spare)
            counts[i] = counts[i] + extra
            spare = spare - extra
    return np.array(counts)


def scatter_about(key, shape, scale, reach, split=(), kind=jnp.bfloat16):
    gain = steps_of(key, shape, split, -0.22, 0.18) if split else 1.0
    drawn = jax.random.normal(key, shape, jnp.float32) * scale * gain
    return jnp.minimum(jnp.maximum(drawn, -reach), reach).astype(kind)


def setup_inputs(seed: int = 0) -> dict:
    seeds = jax.random.split(jax.random.key(seed), 6)
    out_grad = scatter_about(seeds[0], (TOKENS, D), 0.6, 6.0, ((0, 512),))
    expert_ids_keys = jax.random.split(jax.random.fold_in(seeds[1], 1), TOKENS // TOK_DEV)
    expert_ids_turns = jax.random.permutation(jax.random.fold_in(seeds[1], 3), TOKENS // TOK_DEV)
    expert_ids = jax.vmap(lambda own, number: deal_out(jax.random.fold_in(seeds[1], 2), own, number, TOK_DEV, EXPERTS, TOP, CAP, 1))(expert_ids_keys, expert_ids_turns).reshape((TOKENS, TOP))
    route_weights = jnp.clip(jnp.exp(math.log(1.0) - 2.9996462 * jax.random.uniform(seeds[2], (TOKENS, TOP), jnp.float32) ** steps_of(seeds[2], (TOKENS, TOP), ((0, 512),), -0.2, 0.2)), 0.049804688, 1.0).astype(jnp.bfloat16)
    pre_activations = scatter_about(seeds[3], (TOKENS, TOP, 2 * FF), 1.0, 6.0, ((0, 512),))
    down_weight = scatter_about(seeds[4], (EXPERTS, FF, D), FF ** -0.5, 0.21875, ((0, 16), (1, 32)))
    return {"out_grad": out_grad, "expert_ids": expert_ids, "route_weights": route_weights, "pre_activations": pre_activations, "down_weight": down_weight}


def swiglu_value(pre, units):
    gate_val = pre[..., :units].astype(jnp.float32)
    up_val = pre[..., units:].astype(jnp.float32)
    return gate_val * jax.nn.sigmoid(gate_val) * up_val


def swiglu_back(pre, weights, hidden_grad, units):
    gate_val = pre[..., :units].astype(jnp.float32)
    up_val = pre[..., units:].astype(jnp.float32)
    sigmoid_val = jax.nn.sigmoid(gate_val)
    cotangent = weights.astype(jnp.float32)[..., None] * hidden_grad.astype(jnp.float32)
    gate_grad = cotangent * up_val * sigmoid_val * (1.0 + gate_val * (1.0 - sigmoid_val))
    up_grad = cotangent * gate_val * sigmoid_val
    return jnp.concatenate([gate_grad, up_grad], axis=-1).astype(jnp.bfloat16)


def slot_places(chosen):
    flat = chosen.reshape(-1).astype(jnp.int32)
    onehot = (flat[:, None] == jnp.arange(EXPERTS, dtype=jnp.int32)[None, :]).astype(jnp.int32)
    ranks = jnp.cumsum(onehot, axis=0) - 1
    rank = jnp.sum(ranks * onehot, axis=1).astype(jnp.int32)
    target = flat * CAP + rank
    count = flat.shape[0]
    source = jnp.full((EXPERTS * CAP,), count, jnp.int32).at[target].set(jnp.arange(count, dtype=jnp.int32))
    return target, source


def reference(out_grad, expert_ids, route_weights, pre_activations, down_weight):
    units = FF
    group_rows = N_EXPERT * TOK_DEV
    slots = TOK_DEV * TOP
    group_slots = N_EXPERT * slots

    def group_step(total, group):
        start = (group * group_rows).astype(jnp.int32)
        grads = lax.dynamic_slice_in_dim(out_grad, start, group_rows, 0)
        chosen = lax.dynamic_slice_in_dim(expert_ids, start, group_rows, 0)
        weights_g = lax.dynamic_slice_in_dim(route_weights, start, group_rows, 0)
        pre = lax.dynamic_slice_in_dim(pre_activations, start, group_rows, 0)
        targets, sources = jax.vmap(slot_places)(chosen.reshape(N_EXPERT, TOK_DEV, TOP))
        offset = jnp.arange(N_EXPERT, dtype=jnp.int32)[:, None] * slots
        glob = jnp.where(sources < slots, sources + offset, group_slots).astype(jnp.int32)
        glob = glob.reshape(N_EXPERT, EXPERTS, CAP).transpose(1, 0, 2).reshape(EXPERTS, N_EXPERT * CAP)
        pad_grads = jnp.concatenate([grads, jnp.zeros((1, D), grads.dtype)], axis=0)
        pad_pre = jnp.concatenate([pre.reshape(group_slots, 2 * units), jnp.zeros((1, 2 * units), pre.dtype)], axis=0)
        pad_weights = jnp.concatenate([weights_g.reshape(group_slots), jnp.zeros((1,), weights_g.dtype)], axis=0)

        def expert_step(packed):
            index, weight = packed
            grad_rows = pad_grads[index // TOP]
            pre_rows = pad_pre[index]
            weight_rows = pad_weights[index]
            hidden = swiglu_value(pre_rows, units).astype(jnp.bfloat16)
            hidden_grad = jnp.dot(grad_rows, weight.T, preferred_element_type=jnp.float32).astype(jnp.bfloat16)
            scaled = (weight_rows.astype(jnp.float32)[:, None] * grad_rows.astype(jnp.float32)).astype(jnp.bfloat16)
            part = jnp.dot(hidden.T, scaled, preferred_element_type=jnp.float32).astype(jnp.bfloat16)
            pre_part = swiglu_back(pre_rows, weight_rows, hidden_grad, units)
            weight_part = jnp.sum(hidden_grad.astype(jnp.float32) * hidden.astype(jnp.float32), axis=-1).astype(jnp.bfloat16)
            return part, pre_part, weight_part

        parts, pre_parts, weight_parts = lax.map(expert_step, (glob, down_weight))
        parts = lax.optimization_barrier(parts)
        total = total + parts.astype(jnp.float32)
        flat_index = glob.reshape(-1)
        pre_out = jnp.zeros((group_slots + 1, 2 * units), jnp.bfloat16).at[flat_index].set(pre_parts.reshape(-1, 2 * units))
        weight_out = jnp.zeros((group_slots + 1,), jnp.bfloat16).at[flat_index].set(weight_parts.reshape(-1))
        return total, (pre_out[:group_slots].reshape(group_rows, TOP, 2 * units), weight_out[:group_slots].reshape(group_rows, TOP))

    start_total = jnp.zeros((EXPERTS, FF, D), jnp.float32)
    total, outputs = lax.scan(group_step, start_total, jnp.arange(N_DP, dtype=jnp.int32))
    pre_grad = outputs[0].reshape(TOKENS, TOP, 2 * units)
    weight_grad = outputs[1].reshape(TOKENS, TOP)
    down_grad = (total / N_DP).astype(jnp.bfloat16)
    return pre_grad, weight_grad, down_grad
```

```python
import jax
import jax.numpy as jnp
from jax import lax
from jax.sharding import PartitionSpec as P

F32 = jnp.float32
BF16 = jnp.bfloat16


def gather_rows(x):
    return lax.all_gather(x, "dp", axis=0, tiled=True)


def body(out_grad, expert_ids, route_weights, pre_activations, down_weight):
    tok, width = out_grad.shape
    top = expert_ids.shape[1]
    units = pre_activations.shape[2] // 2
    ndp = lax.axis_size("dp")
    rows = down_weight.shape[1]
    n_all = ndp * tok

    w_all = lax.all_gather(down_weight, "expert", axis=0, tiled=True)
    experts = w_all.shape[0]
    wcat = w_all.reshape(experts * rows, width)
    og_all = gather_rows(out_grad)
    ids_t = gather_rows(expert_ids).T
    rw_t = gather_rows(route_weights).T.astype(F32)

    gate = pre_activations[..., :units].astype(F32)
    up = pre_activations[..., units:].astype(F32)
    sig = jax.nn.sigmoid(gate)
    hidden = (gate * sig * up).astype(BF16)

    send_h = hidden.reshape(tok, top, ndp, rows).transpose(2, 0, 1, 3)
    got_h = lax.all_to_all(send_h, "dp", 0, 0, tiled=True)
    hid_t = got_h.transpose(2, 3, 0, 1).reshape(top, rows, n_all).astype(F32)

    eidx = jnp.arange(experts, dtype=jnp.int32)[:, None, None]
    hp = jnp.zeros((experts, rows, n_all), F32)
    for k in range(top):
        hp = hp + jnp.where(ids_t[k][None, None, :] == eidx, (rw_t[k][None, :] * hid_t[k])[None], 0.0)
    hp = hp.reshape(experts * rows, n_all).astype(BF16)
    part = lax.dot_general(hp, og_all, (((1,), (0,)), ((), ())), preferred_element_type=F32)

    r_t = lax.dot_general(wcat, og_all, (((1,), (1,)), ((), ())), preferred_element_type=F32)
    r_t = r_t.reshape(experts, rows, n_all)
    hg_t = jnp.stack(
        [jnp.sum(jnp.where(ids_t[k][None, None, :] == eidx, r_t, 0.0), axis=0) for k in range(top)]
    ).astype(BF16)

    send_g = hg_t.reshape(top, rows, ndp, tok).transpose(2, 3, 0, 1)
    got_g = lax.all_to_all(send_g, "dp", 0, 0, tiled=True)
    hidden_grad = got_g.transpose(1, 2, 0, 3).reshape(tok, top, units)

    hg32 = hidden_grad.astype(F32)
    weight_grad = jnp.sum(hg32 * hidden.astype(F32), axis=-1).astype(BF16)
    cot = route_weights.astype(F32)[..., None] * hg32
    gate_grad = cot * up * sig * (1.0 + gate * (1.0 - sig))
    up_grad = cot * gate * sig
    pre_grad = jnp.concatenate([gate_grad, up_grad], axis=-1).astype(BF16)

    summed = lax.psum_scatter(
        part.reshape(experts, rows, width).astype(BF16), "expert", scatter_dimension=0, tiled=True
    )
    down_grad = (summed.astype(F32) / ndp).astype(BF16)
    return pre_grad, weight_grad, down_grad


def solution(mesh):
    return jax.shard_map(
        body,
        mesh=mesh,
        in_specs=(
            P(("dp", "expert"), None),
            P(("dp", "expert"), None),
            P(("dp", "expert"), None),
            P(("dp", "expert"), None, None),
            P("expert", "dp", None),
        ),
        out_specs=(
            P(("dp", "expert"), None, None),
            P(("dp", "expert"), None),
            P("expert", "dp", None),
        ),
        check_vma=False,
    )
```

```python
import jax
import jax.numpy as jnp
from jax import lax
from jax.sharding import PartitionSpec as P

F32 = jnp.float32
BF16 = jnp.bfloat16


def body(out_grad, expert_ids, route_weights, pre_activations, down_weight):
    tok, width = out_grad.shape
    top = expert_ids.shape[1]
    units = pre_activations.shape[2] // 2
    ndp = lax.axis_size("dp")
    rows = down_weight.shape[1]
    n_all = ndp * tok

    nex = lax.axis_size("expert")
    w_all = lax.all_to_all(
        jnp.broadcast_to(down_weight, (nex,) + down_weight.shape[1:]), "expert", 0, 0, tiled=True
    )
    experts = w_all.shape[0]
    wcat = w_all.reshape(experts * rows, width)
    og_all = lax.all_gather(out_grad, "dp", axis=0, tiled=True)

    gate = pre_activations[..., :units].astype(F32)
    up = pre_activations[..., units:].astype(F32)
    sig = jax.nn.sigmoid(gate)
    hidden = (gate * sig * up).astype(BF16)

    send_h = hidden.reshape(tok, top, ndp, rows).transpose(2, 1, 3, 0)
    meta = jnp.stack([expert_ids.T.astype(BF16), route_weights.T], axis=1)
    send_h = jnp.concatenate([send_h, jnp.broadcast_to(meta[None], (ndp, top, 2, tok))], axis=2)
    got_h = lax.all_to_all(send_h, "dp", 0, 0, tiled=True)
    got_h = got_h.transpose(1, 2, 0, 3).reshape(top, rows + 2, n_all)
    hid_t = got_h[:, :rows].astype(F32)
    ids_t = got_h[:, rows].astype(F32)
    rw_t = got_h[:, rows + 1].astype(F32)

    eidx = jnp.arange(experts, dtype=F32)[:, None, None]
    hp = jnp.zeros((experts, rows, n_all), F32)
    for k in range(top):
        hp = hp + jnp.where(ids_t[k][None, None, :] == eidx, (rw_t[k][None, :] * hid_t[k])[None], 0.0)
    hp = hp.reshape(experts * rows, n_all).astype(BF16)
    part = lax.dot_general(hp, og_all, (((1,), (0,)), ((), ())), preferred_element_type=F32)
    part = part.reshape(experts, rows, width).astype(BF16)
    part, wcat = lax.optimization_barrier((part, wcat))

    r_t = lax.dot_general(wcat, og_all, (((1,), (1,)), ((), ())), preferred_element_type=F32)
    r_t = r_t.reshape(experts, rows, n_all)
    hg_t = jnp.stack(
        [jnp.sum(jnp.where(ids_t[k][None, None, :] == eidx, r_t, 0.0), axis=0) for k in range(top)]
    ).astype(BF16)

    send_g = hg_t.reshape(top, rows, ndp, tok).transpose(2, 0, 1, 3)
    got_g = lax.all_to_all(send_g, "dp", 0, 0, tiled=True)
    hidden_grad = got_g.transpose(3, 1, 0, 2).reshape(tok, top, units)

    hg32 = hidden_grad.astype(F32)
    weight_grad = jnp.sum(hg32 * hidden.astype(F32), axis=-1).astype(BF16)
    cot = route_weights.astype(F32)[..., None] * hg32
    gate_grad = cot * up * sig * (1.0 + gate * (1.0 - sig))
    up_grad = cot * gate * sig
    pre_grad = jnp.concatenate([gate_grad, up_grad], axis=-1).astype(BF16)

    summed = lax.psum_scatter(part, "expert", scatter_dimension=0, tiled=True)
    down_grad = (summed.astype(F32) / ndp).astype(BF16)
    return pre_grad, weight_grad, down_grad


def solution(mesh):
    return jax.shard_map(
        body,
        mesh=mesh,
        in_specs=(
            P(("dp", "expert"), None),
            P(("dp", "expert"), None),
            P(("dp", "expert"), None),
            P(("dp", "expert"), None, None),
            P("expert", "dp", None),
        ),
        out_specs=(
            P(("dp", "expert"), None, None),
            P(("dp", "expert"), None),
            P("expert", "dp", None),
        ),
        check_vma=False,
    )
```

```python
import jax
import jax.numpy as jnp
from jax import lax
from jax.sharding import PartitionSpec as P


F32 = jnp.float32
BF16 = jnp.bfloat16


def layer(out_grad, expert_ids, route_weights, pre_activations, down_weight):
    tok, width = out_grad.shape
    top = expert_ids.shape[1]
    units = pre_activations.shape[2] // 2
    ndp = lax.axis_size("dp")
    rows = down_weight.shape[1]
    n_all = ndp * tok

    nex = lax.axis_size("expert")
    w_all = lax.all_to_all(
        jnp.broadcast_to(down_weight, (nex,) + down_weight.shape[1:]), "expert", 0, 0, tiled=True
    )
    experts = w_all.shape[0]
    wcat = w_all.reshape(experts * rows, width)
    og_all = lax.all_gather(out_grad, "dp", axis=0, tiled=True)

    gate = pre_activations[..., :units].astype(F32)
    up = pre_activations[..., units:].astype(F32)
    sig = jax.nn.sigmoid(gate)
    hidden = (gate * sig * up).astype(BF16)

    send_h = hidden.reshape(tok, top, ndp, rows).transpose(2, 1, 3, 0)
    meta = jnp.stack([expert_ids.T.astype(BF16), route_weights.T], axis=1)
    send_h = jnp.concatenate([send_h, jnp.broadcast_to(meta[None], (ndp, top, 2, tok))], axis=2)
    got_h = lax.all_to_all(send_h, "dp", 0, 0, tiled=True)
    got_h = got_h.transpose(1, 2, 0, 3).reshape(top, rows + 2, n_all)
    hid_t = got_h[:, :rows].astype(F32)
    ids_t = got_h[:, rows].astype(F32)
    rw_t = got_h[:, rows + 1].astype(F32)

    eidx = jnp.arange(experts, dtype=F32)[:, None, None]
    hp = jnp.zeros((experts, rows, n_all), F32)
    for k in range(top):
        hp = hp + jnp.where(ids_t[k][None, None, :] == eidx, (rw_t[k][None, :] * hid_t[k])[None], 0.0)
    hp = hp.reshape(experts * rows, n_all).astype(BF16)
    part = lax.dot_general(hp, og_all, (((1,), (0,)), ((), ())), preferred_element_type=F32)
    part = part.reshape(experts, rows, width).astype(BF16)
    part, wcat = lax.optimization_barrier((part, wcat))

    split = rows // 2
    moved = lax.all_to_all(part[:, :split], "expert", 0, 0, tiled=True)
    second = lax.psum_scatter(part[:, split:], "expert", scatter_dimension=0, tiled=True)

    r_t = lax.dot_general(wcat, og_all, (((1,), (1,)), ((), ())), preferred_element_type=F32)
    r_t = r_t.reshape(experts, rows, n_all)
    hg_t = jnp.stack(
        [jnp.sum(jnp.where(ids_t[k][None, None, :] == eidx, r_t, 0.0), axis=0) for k in range(top)]
    ).astype(BF16)

    send_g = hg_t.reshape(top, rows, ndp, tok).transpose(2, 0, 1, 3)
    got_g = lax.all_to_all(send_g, "dp", 0, 0, tiled=True)
    hidden_grad = got_g.transpose(3, 1, 0, 2).reshape(tok, top, units)

    hg32 = hidden_grad.astype(F32)
    weight_grad = jnp.sum(hg32 * hidden.astype(F32), axis=-1).astype(BF16)
    cot = route_weights.astype(F32)[..., None] * hg32
    gate_grad = cot * up * sig * (1.0 + gate * (1.0 - sig))
    up_grad = cot * gate * sig
    pre_grad = jnp.concatenate([gate_grad, up_grad], axis=-1).astype(BF16)

    first = jnp.sum(moved.astype(F32), axis=0, keepdims=True)
    down_grad = (jnp.concatenate([first, second.astype(F32)], axis=1) / ndp).astype(BF16)
    return pre_grad, weight_grad, down_grad


def solution(mesh):
    return jax.shard_map(
        layer,
        mesh=mesh,
        in_specs=(
            P(("dp", "expert"), None),
            P(("dp", "expert"), None),
            P(("dp", "expert"), None),
            P(("dp", "expert"), None, None),
            P("expert", "dp", None),
        ),
        out_specs=(
            P(("dp", "expert"), None, None),
            P(("dp", "expert"), None),
            P("expert", "dp", None),
        ),
        check_vma=False,
    )
```

```python
import jax
import numpy as np
import jax.numpy as jnp
from jax import lax
from jax.sharding import PartitionSpec as P

F32 = jnp.float32
BF16 = jnp.bfloat16
SIDE = 4


def coords(i):
    return i // (2 * SIDE), (i // 2) % SIDE, i % 2


def index_of(x, y, c):
    return (x % SIDE) * 2 * SIDE + (y % SIDE) * 2 + c


def shift_first(n, s):
    pairs = []
    for i in range(n):
        x, y, c = coords(i)
        pairs.append((i, index_of(x + s, y, c) if c == 0 else index_of(x, y + s, c)))
    return pairs


def shift_second(n, s):
    pairs = []
    for i in range(n):
        x, y, c = coords(i)
        pairs.append((i, index_of(x, y + s, c) if c == 0 else index_of(x + s, y, c)))
    return pairs


def ring_gather(block, n):
    half = block.shape[1] // 2
    up, down = shift_first(n, 1), shift_first(n, -1)
    from_low = lax.ppermute(block, "dp", up)
    from_high = lax.ppermute(block, "dp", down)
    far_left = lax.ppermute(from_low[:, :half], "dp", up)
    far_right = lax.ppermute(from_high[:, half:], "dp", down)
    line = jnp.concatenate(
        [block, from_high, jnp.concatenate([far_left, far_right], axis=1), from_low], axis=0
    )
    up, down = shift_second(n, 1), shift_second(n, -1)
    line_low = lax.ppermute(line, "dp", up)
    line_high = lax.ppermute(line, "dp", down)
    line_far_left = lax.ppermute(line_low[:, :half], "dp", up)
    line_far_right = lax.ppermute(line_high[:, half:], "dp", down)
    mine = [line, line_high, (line_far_left, line_far_right), line_low]
    swap = [(i, i ^ 1) for i in range(n)]
    other = [
        lax.ppermute(line, "dp", swap),
        lax.ppermute(line_high, "dp", swap),
        (lax.ppermute(line_far_left, "dp", swap), lax.ppermute(line_far_right, "dp", swap)),
        lax.ppermute(line_low, "dp", swap),
    ]
    return mine + other


def block_order(n):
    table = np.zeros((n, n), np.int32)
    for i in range(n):
        x, y, c = coords(i)
        out = []
        for cc in (c, 1 - c):
            for db in range(SIDE):
                for da in range(SIDE):
                    out.append(index_of(x + da, y + db, 0) if cc == 0 else index_of(x + db, y + da, 1))
        table[i] = out
    return table


def body(out_grad, expert_ids, route_weights, pre_activations, down_weight):
    tok, width = out_grad.shape
    top = expert_ids.shape[1]
    units = pre_activations.shape[2] // 2
    ndp = lax.axis_size("dp")
    rows = down_weight.shape[1]
    n_all = ndp * tok
    half = width // 2

    w_all = lax.all_gather(down_weight, "expert", axis=0, tiled=True)
    experts = w_all.shape[0]
    wcat = w_all.reshape(experts * rows, width)

    pieces = ring_gather(out_grad, ndp)
    table = block_order(ndp)
    me = lax.axis_index("dp")
    order = jnp.asarray(table)[me]
    inverse = jnp.asarray(np.argsort(table, axis=1).astype(np.int32))[me]

    gate = pre_activations[..., :units].astype(F32)
    up = pre_activations[..., units:].astype(F32)
    sig = jax.nn.sigmoid(gate)
    hidden = (gate * sig * up).astype(BF16)

    send_h = hidden.reshape(tok, top, ndp, rows).transpose(2, 1, 3, 0)
    meta = jnp.stack([expert_ids.T.astype(BF16), route_weights.T], axis=1)
    send_h = jnp.concatenate([send_h, jnp.broadcast_to(meta[None], (ndp, top, 2, tok))], axis=2)
    got_h = lax.all_to_all(send_h, "dp", 0, 0, tiled=True)
    got_h = jnp.take(got_h, order, axis=0)
    got_h = got_h.transpose(1, 2, 0, 3).reshape(top, rows + 2, n_all)
    hid_t = got_h[:, :rows].astype(F32)
    ids_t = got_h[:, rows].astype(F32)
    rw_t = got_h[:, rows + 1].astype(F32)

    eidx = jnp.arange(experts, dtype=F32)[:, None, None]
    hp = jnp.zeros((experts, rows, n_all), F32)
    for k in range(top):
        hp = hp + jnp.where(ids_t[k][None, None, :] == eidx, (rw_t[k][None, :] * hid_t[k])[None], 0.0)
    hp = hp.reshape(experts * rows, n_all).astype(BF16)

    def tn(a, b):
        return lax.dot_general(a, b, (((1,), (0,)), ((), ())), preferred_element_type=F32)

    def nt(a, b):
        return lax.dot_general(a, b, (((1,), (1,)), ((), ())), preferred_element_type=F32)

    part = jnp.zeros((experts * rows, width), F32)
    part_left = jnp.zeros((experts * rows, half), F32)
    part_right = jnp.zeros((experts * rows, half), F32)
    start = 0
    for piece in pieces:
        if isinstance(piece, tuple):
            left, right = piece
            count = left.shape[0]
            cols = hp[:, start : start + count]
            part_left = part_left + tn(cols, left)
            part_right = part_right + tn(cols, right)
        else:
            count = piece.shape[0]
            part = part + tn(hp[:, start : start + count], piece)
        start += count
    part = part + jnp.concatenate([part_left, part_right], axis=1)
    part = part.reshape(experts, rows, width).astype(BF16)
    part, wcat = lax.optimization_barrier((part, wcat))

    r_list = []
    for piece in pieces:
        if isinstance(piece, tuple):
            left, right = piece
            r_list.append(nt(wcat[:, :half], left) + nt(wcat[:, half:], right))
        else:
            r_list.append(nt(wcat, piece))
    r_t = jnp.concatenate(r_list, axis=1).reshape(experts, rows, n_all)
    hg_t = jnp.stack(
        [jnp.sum(jnp.where(ids_t[k][None, None, :] == eidx, r_t, 0.0), axis=0) for k in range(top)]
    ).astype(BF16)

    send_g = hg_t.reshape(top, rows, ndp, tok).transpose(2, 0, 1, 3)
    send_g = jnp.take(send_g, inverse, axis=0)
    got_g = lax.all_to_all(send_g, "dp", 0, 0, tiled=True)
    hidden_grad = got_g.transpose(3, 1, 0, 2).reshape(tok, top, units)

    hg32 = hidden_grad.astype(F32)
    weight_grad = jnp.sum(hg32 * hidden.astype(F32), axis=-1).astype(BF16)
    cot = route_weights.astype(F32)[..., None] * hg32
    gate_grad = cot * up * sig * (1.0 + gate * (1.0 - sig))
    up_grad = cot * gate * sig
    pre_grad = jnp.concatenate([gate_grad, up_grad], axis=-1).astype(BF16)

    summed = lax.psum_scatter(part, "expert", scatter_dimension=0, tiled=True)
    down_grad = (summed.astype(F32) / ndp).astype(BF16)
    return pre_grad, weight_grad, down_grad


def solution(mesh):
    return jax.shard_map(
        body,
        mesh=mesh,
        in_specs=(
            P(("dp", "expert"), None),
            P(("dp", "expert"), None),
            P(("dp", "expert"), None),
            P(("dp", "expert"), None, None),
            P("expert", "dp", None),
        ),
        out_specs=(
            P(("dp", "expert"), None, None),
            P(("dp", "expert"), None),
            P("expert", "dp", None),
        ),
        check_vma=False,
    )
```

```python
import jax
import numpy as np
import jax.numpy as jnp
from jax import lax
from jax.sharding import Mesh, PartitionSpec as P

PLANE = ("mx", "my", "mc")

F32 = jnp.float32
BF16 = jnp.bfloat16


def body(out_grad, expert_ids, route_weights, pre_activations, down_weight):
    tok, width = out_grad.shape
    top = expert_ids.shape[1]
    units = pre_activations.shape[2] // 2
    ndp = lax.axis_size(PLANE)
    rows = down_weight.shape[1]
    n_all = ndp * tok

    nex = lax.axis_size("expert")
    w_all = lax.all_to_all(
        jnp.broadcast_to(down_weight, (nex,) + down_weight.shape[1:]), "expert", 0, 0, tiled=True
    )
    experts = w_all.shape[0]
    wcat = w_all.reshape(experts * rows, width)
    core = lax.axis_index("mc")
    og_mine = lax.all_gather(out_grad, ("mx", "my"), axis=0, tiled=True)
    og_other = lax.ppermute(og_mine, "mc", [(0, 1), (1, 0)])
    nhalf = og_mine.shape[0]
    table = np.stack([np.concatenate([np.arange(ndp // 2) * 2 + c, np.arange(ndp // 2) * 2 + 1 - c]) for c in (0, 1)])
    order = jnp.asarray(table.astype(np.int32))[core]
    inverse = jnp.asarray(np.argsort(table, axis=1).astype(np.int32))[core]

    gate = pre_activations[..., :units].astype(F32)
    up = pre_activations[..., units:].astype(F32)
    sig = jax.nn.sigmoid(gate)
    hidden = (gate * sig * up).astype(BF16)

    send_h = hidden.reshape(tok, top, ndp, rows).transpose(2, 1, 3, 0)
    meta = jnp.stack([expert_ids.T.astype(BF16), route_weights.T], axis=1)
    send_h = jnp.concatenate([send_h, jnp.broadcast_to(meta[None], (ndp, top, 2, tok))], axis=2)
    got_h = lax.all_to_all(send_h, PLANE, 0, 0, tiled=True)
    got_h = jnp.take(got_h, order, axis=0)
    got_h = got_h.transpose(1, 2, 0, 3).reshape(top, rows + 2, n_all)
    hid_t = got_h[:, :rows].astype(F32)
    ids_t = got_h[:, rows].astype(F32)
    rw_t = got_h[:, rows + 1].astype(F32)

    eidx = jnp.arange(experts, dtype=F32)[:, None, None]
    hp = jnp.zeros((experts, rows, n_all), F32)
    for k in range(top):
        hp = hp + jnp.where(ids_t[k][None, None, :] == eidx, (rw_t[k][None, :] * hid_t[k])[None], 0.0)
    hp = hp.reshape(experts * rows, n_all).astype(BF16)
    part = lax.dot_general(hp[:, :nhalf], og_mine, (((1,), (0,)), ((), ())), preferred_element_type=F32)
    part = part + lax.dot_general(hp[:, nhalf:], og_other, (((1,), (0,)), ((), ())), preferred_element_type=F32)
    part = part.reshape(experts, rows, width).astype(BF16)
    part, wcat = lax.optimization_barrier((part, wcat))

    r_t = jnp.concatenate(
        [lax.dot_general(wcat, og, (((1,), (1,)), ((), ())), preferred_element_type=F32) for og in (og_mine, og_other)],
        axis=1,
    )
    r_t = r_t.reshape(experts, rows, n_all)
    hg_t = jnp.stack(
        [jnp.sum(jnp.where(ids_t[k][None, None, :] == eidx, r_t, 0.0), axis=0) for k in range(top)]
    ).astype(BF16)

    send_g = hg_t.reshape(top, rows, ndp, tok).transpose(2, 0, 1, 3)
    send_g = jnp.take(send_g, inverse, axis=0)
    got_g = lax.all_to_all(send_g, PLANE, 0, 0, tiled=True)
    hidden_grad = got_g.transpose(3, 1, 0, 2).reshape(tok, top, units)

    hg32 = hidden_grad.astype(F32)
    weight_grad = jnp.sum(hg32 * hidden.astype(F32), axis=-1).astype(BF16)
    cot = route_weights.astype(F32)[..., None] * hg32
    gate_grad = cot * up * sig * (1.0 + gate * (1.0 - sig))
    up_grad = cot * gate * sig
    pre_grad = jnp.concatenate([gate_grad, up_grad], axis=-1).astype(BF16)

    summed = lax.psum_scatter(part, "expert", scatter_dimension=0, tiled=True)
    down_grad = (summed.astype(F32) / ndp).astype(BF16)
    return pre_grad, weight_grad, down_grad


def solution(mesh):
    side = 4
    plane = Mesh(
        mesh.devices.reshape(side, mesh.devices.shape[0] // (2 * side), 2, mesh.devices.shape[1]),
        PLANE + ("expert",),
    )
    tokens = (PLANE + ("expert",),)
    return jax.shard_map(
        body,
        mesh=plane,
        in_specs=(
            P(tokens[0], None),
            P(tokens[0], None),
            P(tokens[0], None),
            P(tokens[0], None, None),
            P("expert", PLANE, None),
        ),
        out_specs=(
            P(tokens[0], None, None),
            P(tokens[0], None),
            P("expert", PLANE, None),
        ),
        check_vma=False,
    )
```

```python
import jax
import numpy as np
import jax.numpy as jnp
from jax import lax
from jax.sharding import PartitionSpec as P

F32 = jnp.float32
BF16 = jnp.bfloat16
SIDE = 4


def coords(i):
    return i // (2 * SIDE), (i // 2) % SIDE, i % 2


def index_of(x, y, c):
    return (x % SIDE) * 2 * SIDE + (y % SIDE) * 2 + c


def shift_first(n, s):
    pairs = []
    for i in range(n):
        x, y, c = coords(i)
        pairs.append((i, index_of(x + s, y, c) if c == 0 else index_of(x, y + s, c)))
    return pairs


def shift_second(n, s):
    pairs = []
    for i in range(n):
        x, y, c = coords(i)
        pairs.append((i, index_of(x, y + s, c) if c == 0 else index_of(x + s, y, c)))
    return pairs


def ring_gather(block, n):
    half = block.shape[1] // 2

    def spread(piece, shift):
        return (
            lax.ppermute(piece, "dp", shift(n, 1)),
            lax.ppermute(piece, "dp", shift(n, -1)),
            lax.ppermute(piece[:, :half], "dp", shift(n, 2)),
            lax.ppermute(piece[:, half:], "dp", shift(n, -2)),
        )

    low, high, far_left, far_right = spread(block, shift_first)
    line = jnp.concatenate([block, high, jnp.concatenate([far_left, far_right], axis=1), low], axis=0)
    line_low, line_high, line_far_left, line_far_right = spread(line, shift_second)
    mine = [line, line_high, (line_far_left, line_far_right), line_low]
    swap = [(i, i ^ 1) for i in range(n)]
    other = [
        lax.ppermute(line, "dp", swap),
        lax.ppermute(line_high, "dp", swap),
        (lax.ppermute(line_far_left, "dp", swap), lax.ppermute(line_far_right, "dp", swap)),
        lax.ppermute(line_low, "dp", swap),
    ]
    return mine + other


def block_order(n):
    table = np.zeros((n, n), np.int32)
    for i in range(n):
        x, y, c = coords(i)
        out = []
        for cc in (c, 1 - c):
            for db in range(SIDE):
                for da in range(SIDE):
                    out.append(index_of(x + da, y + db, 0) if cc == 0 else index_of(x + db, y + da, 1))
        table[i] = out
    return table


def body(out_grad, expert_ids, route_weights, pre_activations, down_weight):
    tok, width = out_grad.shape
    top = expert_ids.shape[1]
    units = pre_activations.shape[2] // 2
    ndp = lax.axis_size("dp")
    rows = down_weight.shape[1]
    n_all = ndp * tok
    half = width // 2

    nex = lax.axis_size("expert")
    w_all = lax.all_to_all(
        jnp.broadcast_to(down_weight, (nex,) + down_weight.shape[1:]), "expert", 0, 0, tiled=True
    )
    experts = w_all.shape[0]
    wcat = w_all.reshape(experts * rows, width)

    pieces = ring_gather(out_grad, ndp)
    table = block_order(ndp)
    me = lax.axis_index("dp")
    order = jnp.asarray(table)[me]
    inverse = jnp.asarray(np.argsort(table, axis=1).astype(np.int32))[me]

    gate = pre_activations[..., :units].astype(F32)
    up = pre_activations[..., units:].astype(F32)
    sig = jax.nn.sigmoid(gate)
    hidden = (gate * sig * up).astype(BF16)

    send_h = hidden.reshape(tok, top, ndp, rows).transpose(2, 1, 3, 0)
    meta = jnp.stack([expert_ids.T.astype(BF16), route_weights.T], axis=1)
    send_h = jnp.concatenate([send_h, jnp.broadcast_to(meta[None], (ndp, top, 2, tok))], axis=2)
    got_h = lax.all_to_all(send_h, "dp", 0, 0, tiled=True)
    got_h = jnp.take(got_h, order, axis=0)
    got_h = got_h.transpose(1, 2, 0, 3).reshape(top, rows + 2, n_all)
    hid_t = got_h[:, :rows].astype(F32)
    ids_t = got_h[:, rows].astype(F32)
    rw_t = got_h[:, rows + 1].astype(F32)

    eidx = jnp.arange(experts, dtype=F32)[:, None, None]
    hp = jnp.zeros((experts, rows, n_all), F32)
    for k in range(top):
        hp = hp + jnp.where(ids_t[k][None, None, :] == eidx, (rw_t[k][None, :] * hid_t[k])[None], 0.0)
    hp = hp.reshape(experts * rows, n_all).astype(BF16)

    def tn(a, b):
        return lax.dot_general(a, b, (((1,), (0,)), ((), ())), preferred_element_type=F32)

    def nt(a, b):
        return lax.dot_general(a, b, (((1,), (1,)), ((), ())), preferred_element_type=F32)

    part = jnp.zeros((experts * rows, width), F32)
    part_left = jnp.zeros((experts * rows, half), F32)
    part_right = jnp.zeros((experts * rows, half), F32)
    start = 0
    for piece in pieces:
        if isinstance(piece, tuple):
            left, right = piece
            count = left.shape[0]
            cols = hp[:, start : start + count]
            part_left = part_left + tn(cols, left)
            part_right = part_right + tn(cols, right)
        else:
            count = piece.shape[0]
            part = part + tn(hp[:, start : start + count], piece)
        start += count
    part = part + jnp.concatenate([part_left, part_right], axis=1)
    part = part.reshape(experts, rows, width).astype(BF16)
    part, wcat = lax.optimization_barrier((part, wcat))

    r_list = []
    for piece in pieces:
        if isinstance(piece, tuple):
            left, right = piece
            r_list.append(nt(wcat[:, :half], left) + nt(wcat[:, half:], right))
        else:
            r_list.append(nt(wcat, piece))
    r_t = jnp.concatenate(r_list, axis=1).reshape(experts, rows, n_all)
    hg_t = jnp.stack(
        [jnp.sum(jnp.where(ids_t[k][None, None, :] == eidx, r_t, 0.0), axis=0) for k in range(top)]
    ).astype(BF16)

    send_g = hg_t.reshape(top, rows, ndp, tok).transpose(2, 0, 1, 3)
    send_g = jnp.take(send_g, inverse, axis=0)
    got_g = lax.all_to_all(send_g, "dp", 0, 0, tiled=True)
    hidden_grad = got_g.transpose(3, 1, 0, 2).reshape(tok, top, units)

    hg32 = hidden_grad.astype(F32)
    weight_grad = jnp.sum(hg32 * hidden.astype(F32), axis=-1).astype(BF16)
    cot = route_weights.astype(F32)[..., None] * hg32
    gate_grad = cot * up * sig * (1.0 + gate * (1.0 - sig))
    up_grad = cot * gate * sig
    pre_grad = jnp.concatenate([gate_grad, up_grad], axis=-1).astype(BF16)

    summed = lax.psum_scatter(part, "expert", scatter_dimension=0, tiled=True)
    down_grad = (summed.astype(F32) / ndp).astype(BF16)
    return pre_grad, weight_grad, down_grad


def solution(mesh):
    return jax.shard_map(
        body,
        mesh=mesh,
        in_specs=(
            P(("dp", "expert"), None),
            P(("dp", "expert"), None),
            P(("dp", "expert"), None),
            P(("dp", "expert"), None, None),
            P("expert", "dp", None),
        ),
        out_specs=(
            P(("dp", "expert"), None, None),
            P(("dp", "expert"), None),
            P("expert", "dp", None),
        ),
        check_vma=False,
    )
```

```python
import jax
import jax.numpy as jnp
from jax import lax
from jax.sharding import PartitionSpec as P

F32 = jnp.float32
BF16 = jnp.bfloat16


def body(out_grad, expert_ids, route_weights, pre_activations, down_weight):
    tok, width = out_grad.shape
    top = expert_ids.shape[1]
    units = pre_activations.shape[2] // 2
    ndp = lax.axis_size("dp")
    rows = down_weight.shape[1]
    n_all = ndp * tok

    nex = lax.axis_size("expert")
    w_all = lax.all_to_all(
        jnp.broadcast_to(down_weight, (nex,) + down_weight.shape[1:]), "expert", 0, 0, tiled=True
    )
    experts = w_all.shape[0]
    wcat = w_all.reshape(experts * rows, width)
    og_all = lax.all_gather(out_grad, "dp", axis=0, tiled=True)

    gate = pre_activations[..., :units].astype(F32)
    up = pre_activations[..., units:].astype(F32)
    sig = jax.nn.sigmoid(gate)
    hidden = (gate * sig * up).astype(BF16)

    send_h = hidden.reshape(tok, top, ndp, rows).transpose(2, 1, 3, 0)
    meta = jnp.stack([expert_ids.T.astype(BF16), route_weights.T], axis=1)
    send_h = jnp.concatenate([send_h, jnp.broadcast_to(meta[None], (ndp, top, 2, tok))], axis=2)
    got_h = lax.all_to_all(send_h, "dp", 0, 0, tiled=True)
    got_h = got_h.transpose(1, 2, 0, 3).reshape(top, rows + 2, n_all)
    hid_t = got_h[:, :rows].astype(F32)
    ids_t = got_h[:, rows].astype(F32)
    rw_t = got_h[:, rows + 1].astype(F32)

    eidx = jnp.arange(experts, dtype=F32)[:, None, None]
    hp = jnp.zeros((experts, rows, n_all), F32)
    for k in range(top):
        hp = hp + jnp.where(ids_t[k][None, None, :] == eidx, (rw_t[k][None, :] * hid_t[k])[None], 0.0)
    hp = hp.reshape(experts * rows, n_all).astype(BF16)
    part = lax.dot_general(hp, og_all, (((1,), (0,)), ((), ())), preferred_element_type=F32)
    part = (part / ndp).reshape(experts, rows, width).astype(BF16)
    down_grad = lax.psum_scatter(part, "expert", scatter_dimension=0, tiled=True)
    _, wcat = lax.optimization_barrier((part, wcat))

    r_t = lax.dot_general(wcat, og_all, (((1,), (1,)), ((), ())), preferred_element_type=F32)
    r_t = r_t.reshape(experts, rows, n_all)
    hg_t = jnp.stack(
        [jnp.sum(jnp.where(ids_t[k][None, None, :] == eidx, r_t, 0.0), axis=0) for k in range(top)]
    ).astype(BF16)

    send_g = hg_t.reshape(top, rows, ndp, tok).transpose(2, 0, 1, 3)
    got_g = lax.all_to_all(send_g, "dp", 0, 0, tiled=True)
    hidden_grad = got_g.transpose(3, 1, 0, 2).reshape(tok, top, units)

    hg32 = hidden_grad.astype(F32)
    weight_grad = jnp.sum(hg32 * hidden.astype(F32), axis=-1).astype(BF16)
    cot = route_weights.astype(F32)[..., None] * hg32
    gate_grad = cot * up * sig * (1.0 + gate * (1.0 - sig))
    up_grad = cot * gate * sig
    pre_grad = jnp.concatenate([gate_grad, up_grad], axis=-1).astype(BF16)

    return pre_grad, weight_grad, down_grad


def solution(mesh):
    return jax.shard_map(
        body,
        mesh=mesh,
        in_specs=(
            P(("dp", "expert"), None),
            P(("dp", "expert"), None),
            P(("dp", "expert"), None),
            P(("dp", "expert"), None, None),
            P("expert", "dp", None),
        ),
        out_specs=(
            P(("dp", "expert"), None, None),
            P(("dp", "expert"), None),
            P("expert", "dp", None),
        ),
        check_vma=False,
    )
```

```python
import jax
import jax.numpy as jnp
from jax import lax
from jax.sharding import PartitionSpec as P

F32 = jnp.float32
BF16 = jnp.bfloat16


def body(out_grad, expert_ids, route_weights, pre_activations, down_weight):
    tok, width = out_grad.shape
    top = expert_ids.shape[1]
    units = pre_activations.shape[2] // 2
    ndp = lax.axis_size("dp")
    rows = down_weight.shape[1]
    n_all = ndp * tok

    nex = lax.axis_size("expert")
    w_all = lax.all_to_all(
        jnp.broadcast_to(down_weight, (nex,) + down_weight.shape[1:]), "expert", 0, 0, tiled=True
    )
    experts = w_all.shape[0]
    wcat = w_all.reshape(experts * rows, width)
    og_all = lax.all_gather(out_grad, "dp", axis=0, tiled=True)

    gate = pre_activations[..., :units].astype(F32)
    up = pre_activations[..., units:].astype(F32)
    sig = jax.nn.sigmoid(gate)
    hidden = (gate * sig * up).astype(BF16)

    send_h = hidden.reshape(tok, top, ndp, rows).transpose(2, 1, 3, 0)
    meta = jnp.stack([expert_ids.T.astype(BF16), route_weights.T], axis=1)
    send_h = jnp.concatenate([send_h, jnp.broadcast_to(meta[None], (ndp, top, 2, tok))], axis=2)
    got_h = lax.all_to_all(send_h, "dp", 0, 0, tiled=True)
    got_h = got_h.transpose(1, 2, 0, 3).reshape(top, rows + 2, n_all)
    hid_t = got_h[:, :rows].astype(F32)
    ids_t = got_h[:, rows].astype(F32)
    rw_t = got_h[:, rows + 1].astype(F32)

    eidx = jnp.arange(experts, dtype=F32)[:, None, None]
    hp = jnp.zeros((experts, rows, n_all), F32)
    for k in range(top):
        hp = hp + jnp.where(ids_t[k][None, None, :] == eidx, (rw_t[k][None, :] * hid_t[k])[None], 0.0)
    hp = hp.reshape(experts * rows, n_all).astype(BF16)
    part = lax.dot_general(hp, og_all, (((1,), (0,)), ((), ())), preferred_element_type=F32)
    part = (part / ndp).reshape(experts, rows, width).astype(BF16)
    dense = part.reshape(experts, 2 * rows, width // 2)
    dense, og_all = lax.optimization_barrier((dense, og_all))
    down_grad = lax.psum_scatter(dense, "expert", scatter_dimension=0, tiled=True).reshape(1, rows, width)

    r_t = lax.dot_general(wcat, og_all, (((1,), (1,)), ((), ())), preferred_element_type=F32)
    r_t = r_t.reshape(experts, rows, n_all)
    hg_t = jnp.stack(
        [jnp.sum(jnp.where(ids_t[k][None, None, :] == eidx, r_t, 0.0), axis=0) for k in range(top)]
    ).astype(BF16)

    send_g = hg_t.reshape(top, rows, ndp, tok).transpose(2, 0, 1, 3)
    got_g = lax.all_to_all(send_g, "dp", 0, 0, tiled=True)
    hidden_grad = got_g.transpose(3, 1, 0, 2).reshape(tok, top, units)

    hg32 = hidden_grad.astype(F32)
    weight_grad = jnp.sum(hg32 * hidden.astype(F32), axis=-1).astype(BF16)
    cot = route_weights.astype(F32)[..., None] * hg32
    gate_grad = cot * up * sig * (1.0 + gate * (1.0 - sig))
    up_grad = cot * gate * sig
    pre_grad = jnp.concatenate([gate_grad, up_grad], axis=-1).astype(BF16)

    return pre_grad, weight_grad, down_grad


def solution(mesh):
    return jax.shard_map(
        body,
        mesh=mesh,
        in_specs=(
            P(("dp", "expert"), None),
            P(("dp", "expert"), None),
            P(("dp", "expert"), None),
            P(("dp", "expert"), None, None),
            P("expert", "dp", None),
        ),
        out_specs=(
            P(("dp", "expert"), None, None),
            P(("dp", "expert"), None),
            P("expert", "dp", None),
        ),
        check_vma=False,
    )
```
